256 devices in a mesh: expert: 128 (over z, x, y), dp: 2 (over core).
Axes of the slice: x: 4, y: 4, z: 8, core: 2. Of those that a mesh axis runs over, the one named last changes fastest.
Arguments:
- hidden: bfloat16 [32768, 8, 1024], P(('expert', 'dp')), may hold values from -8 to 8
- routes: int32 [32768, 8], P(('expert', 'dp')), may hold values from 0 to 127, as said below
- slots: int32 [32768, 8], P(('expert', 'dp')), may hold values from 0 to 15, as said below
- down_weight: bfloat16 [128, 1024, 7168], P('expert', None, 'dp'), may hold values from -0.1875 to 0.1875
- omega: bfloat16 [128, 1024, 256], P('expert'), may hold values from -0.1875 to 0.1875
Outputs:
- whitening: float32 [128, 1024, 1024], P('expert', 'dp')
- basis: float32 [2, 3584, 256], P('dp', 'expert')
The draws below stay inside these ranges and needn't reach their ends.
Inputs may be any that keep to these rules, and one draw needn't show every extreme that they name: `routes`: each token names 8 different experts. Among the tokens of one device no expert is named more than 16 times, and one expert is named exactly 16 times by the tokens of every device. Among the tokens of one device, the pairs that name one expert have different slots.
All inputs are finite; a program needn't handle non-finite values.
Results may differ from the reference program's by a relative error of at most 0.0032.
Values may be sent and summed in bfloat16 or wider, within the bound.
No kernel may reach another device: no remote copies, remote signals or barrier semaphores. Data moves between devices by JAX's collectives and lax.ppermute only.
A program may use at most 128 MiB of HBM per device.

```python
import math
import jax
import jax.numpy as jnp
from jax import lax

D = 7168
TOP = 8
FFW = 1024
R = 256
TOK_DEV = 128
EXPERTS = 128
CAP = 16
TOKENS = 32768
N_DP = 2
DEVICES = 256


def route_table(key):
    hot_expert = jax.random.randint(jax.random.fold_in(key, 7), (), 0, EXPERTS)
    levels = jax.random.randint(jax.random.fold_in(key, 8), (EXPERTS,), 0, 4)
    levels = jnp.where(jnp.arange(EXPERTS) == hot_expert, 12, levels)
    n_cells = EXPERTS * CAP
    n_pairs = TOK_DEV * TOP

    def one_device(dev_index):
        dev_key = jax.random.fold_in(jax.random.fold_in(key, 100), dev_index)
        noise = jax.random.randint(jax.random.fold_in(dev_key, 1), (EXPERTS, CAP), 0, 1024)
        scores = (levels[:, None] * 256 + noise) * n_cells + jnp.arange(n_cells, dtype=jnp.int32).reshape(EXPERTS, CAP)
        picked_vals, picked = lax.top_k(scores.reshape(-1), n_pairs)
        picked = jnp.sort(picked)
        expert_of = picked // CAP
        slot_of = picked % CAP
        position = jnp.arange(n_pairs, dtype=jnp.int32)
        token_perm = jax.random.permutation(jax.random.fold_in(dev_key, 2), TOK_DEV)
        token_of = token_perm[position % TOK_DEV]
        col_keys = jax.random.randint(jax.random.fold_in(dev_key, 3), (TOK_DEV, TOP), 0, 1 << 20) * TOP + jnp.arange(TOP, dtype=jnp.int32)[None, :]
        col_perm = jnp.argsort(col_keys, axis=1).astype(jnp.int32)
        route_of = col_perm[token_of, position // TOK_DEV]
        expert_table = jnp.zeros((TOK_DEV, TOP), jnp.int32).at[token_of, route_of].set(expert_of)
        slot_table = jnp.zeros((TOK_DEV, TOP), jnp.int32).at[token_of, route_of].set(slot_of)
        return (expert_table, slot_table)
    expert_all, slot_all = jax.vmap(one_device)(jnp.arange(DEVICES, dtype=jnp.int32))
    return (expert_all.reshape(TOKENS, TOP), slot_all.reshape(TOKENS, TOP))


def draw_routes(key, part):
    return route_table(key)[0]


def draw_slots(key, part):
    return route_table(key)[1]


def draw_hidden(key, part):
    col_scale = jnp.exp(jax.random.uniform(jax.random.fold_in(key, 11), (FFW,), jnp.float32, jnp.log(0.3), jnp.log(3.0)))
    row_scale = jnp.exp(jax.random.uniform(jax.random.fold_in(key, 12), (TOKENS, TOP, 1), jnp.float32, jnp.log(0.3), jnp.log(3.0)))
    base = jax.random.normal(jax.random.fold_in(key, 13), (TOKENS, TOP, FFW), jnp.float32)
    values = jnp.clip(base * col_scale * row_scale, -8.0, 8.0)
    return values.astype(jnp.bfloat16)


def level_of(key, shape, split, low, largest):
    gain, own = 1.0, jax.random.fold_in(key, 6)
    for dim, blocks in split:
        steps = jnp.exp(jax.random.uniform(jax.random.fold_in(own, dim), (blocks,), jnp.float32, low / len(split), largest / len(split)))
        gain = gain * jnp.repeat(steps, shape[dim] // blocks).reshape([-1 if axis == dim else 1 for axis in range(len(shape))])
    return gain


def gaussian(rng, extent, deviation, limit, cuts=(), kind=jnp.bfloat16):
    array = jax.random.normal(rng, extent, jnp.float32) * deviation
    if len(cuts) > 0:
        array = level_of(rng, extent, cuts, -0.22, 0.18) * array
    return jnp.clip(array, min=-limit, max=limit).astype(kind)


def setup_inputs(seed: int = 0) -> dict:
    arg_keys = jax.random.split(jax.random.key(seed), 6)
    return {
        "hidden": draw_hidden(jax.random.fold_in(arg_keys[5], 71), 0),
        "routes": draw_routes(jax.random.fold_in(arg_keys[5], 71), 0),
        "slots": draw_slots(jax.random.fold_in(arg_keys[5], 71), 0),
        "down_weight": gaussian(arg_keys[3], (EXPERTS, FFW, D), FFW ** -0.5, 0.1875, ((0, 128), (2, 2))),
        "omega": gaussian(arg_keys[4], (EXPERTS, FFW, R), FFW ** -0.5, 0.1875, ((0, 128),)),
    }


damping = 0.1
jitter = 1e-06

def reference(hidden, routes, slots, down_weight, omega):
    n_slot = DEVICES * CAP
    source_dev = (jnp.arange(TOKENS, dtype=jnp.int32) // TOK_DEV).astype(jnp.int32)[:, None]
    slot_index = (routes * n_slot + source_dev * CAP + slots).astype(jnp.int32).reshape(-1)
    buffer = jnp.zeros((EXPERTS * n_slot, FFW), jnp.bfloat16)
    buffer = buffer.at[slot_index].set(hidden.reshape(-1, FFW)).reshape(EXPERTS, n_slot, FFW)
    identity_mat = jnp.eye(FFW, dtype=jnp.float32)

    def per_expert(running, per_items):
        slot_block, down_mat, test_in = per_items
        gram_mat = lax.dot_general(slot_block.astype(jnp.float32), slot_block.astype(jnp.float32), (((0,), (0,)), ((), ())), preferred_element_type=jnp.float32) / n_slot
        damped = gram_mat + (damping * jnp.mean(jnp.diagonal(gram_mat)) + jitter) * identity_mat
        whitening = jnp.linalg.cholesky(damped)
        test_mat = jnp.dot(whitening, test_in.astype(jnp.float32), precision=lax.Precision.HIGHEST).astype(jnp.bfloat16)
        sketch_term = lax.dot_general(down_mat.astype(jnp.float32), test_mat.astype(jnp.float32), (((0,), (0,)), ((), ())), preferred_element_type=jnp.float32)
        return (running + sketch_term, whitening)
    sketch, whitening = lax.scan(per_expert, jnp.zeros((D, R), jnp.float32), (buffer, down_weight, omega))
    small_gram = jnp.dot(sketch.T, sketch, precision=lax.Precision.HIGHEST)
    qr_factor = jnp.linalg.cholesky(small_gram)
    basis_rows = jax.scipy.linalg.solve_triangular(qr_factor, sketch.T, lower=True).T * math.sqrt(D)
    return (whitening, basis_rows.reshape(N_DP, D // N_DP, R))
```

```python
import math

import jax
import jax.numpy as jnp
from jax import lax
from jax.sharding import PartitionSpec as P

damping = 0.1
jitter = 1e-06


def contract(left, right):
    return lax.dot_general(
        left, right, (((0,), (0,)), ((), ())), preferred_element_type=jnp.float32
    )


def local(hidden, routes, slots, down_weight, omega):
    n_exp = lax.axis_size("expert")
    n_dp = lax.axis_size("dp")
    tok_rows, n_route, hid_width = hidden.shape
    capacity = 2 * tok_rows * n_route // n_exp
    n_slot = n_exp * n_dp * capacity
    slot_index = (routes * capacity + slots).reshape(-1)
    outgoing = jnp.zeros((n_exp * capacity, hid_width), jnp.bfloat16)
    outgoing = (
        outgoing.at[slot_index]
        .set(hidden.reshape(-1, hid_width))
        .reshape(n_exp, capacity, hid_width)
    )
    received = lax.all_to_all(outgoing, "expert", split_axis=0, concat_axis=0, tiled=True).reshape(
        n_exp * capacity, hid_width
    )
    partner = lax.ppermute(received, "dp", [(0, 1), (1, 0)])
    gram_mat = (contract(received, received) + contract(partner, partner)) / n_slot
    on_diag = lax.broadcasted_iota(jnp.int32, gram_mat.shape, 0) == lax.broadcasted_iota(
        jnp.int32, gram_mat.shape, 1
    )
    diag_mean = jnp.sum(jnp.where(on_diag, gram_mat, 0.0)) / hid_width
    damped = jnp.where(on_diag, gram_mat + (damping * diag_mean + jitter), gram_mat)
    whitening = jnp.linalg.cholesky(damped)
    test_mat = jnp.dot(
        whitening, omega[0].astype(jnp.float32), precision=lax.Precision.HIGHEST
    ).astype(jnp.bfloat16)
    down_half = down_weight[0]
    half_cols = down_half.shape[1]
    term = contract(down_half, test_mat).reshape(n_exp, half_cols // n_exp, -1)
    sketch = lax.psum_scatter(term, "expert", scatter_dimension=0, tiled=True)[0]
    small_gram = lax.psum(
        jnp.dot(sketch.T, sketch, precision=lax.Precision.HIGHEST), ("expert", "dp")
    )
    qr_factor = jnp.linalg.cholesky(small_gram)
    basis_rows = jax.scipy.linalg.solve_triangular(qr_factor, sketch.T, lower=True).T * math.sqrt(
        half_cols * n_dp
    )
    own_rows = lax.dynamic_slice_in_dim(
        whitening, lax.axis_index("dp") * (hid_width // n_dp), hid_width // n_dp, 0
    )
    return (own_rows[None], basis_rows[None])


def solution(mesh):
    placed = (
        P(("expert", "dp"), None, None),
        P(("expert", "dp"), None),
        P(("expert", "dp"), None),
        P("expert", None, "dp"),
        P("expert", None, None),
    )
    return jax.shard_map(
        local,
        mesh=mesh,
        in_specs=placed,
        out_specs=(P("expert", "dp", None), P("dp", "expert", None)),
        check_vma=False,
    )
```

```python
import math

import jax
import jax.numpy as jnp
from jax import lax
from jax.sharding import PartitionSpec as P

damping = 0.1
jitter = 1e-06


def contract(left, right):
    return lax.dot_general(
        left, right, (((0,), (0,)), ((), ())), preferred_element_type=jnp.float32
    )


def xor_pairs(n, mask):
    return [(i, i ^ mask) for i in range(n)]


def scatter_sum(term, orders):
    n_exp, rows, cols = term.shape
    n_bits = n_exp.bit_length() - 1
    me = lax.axis_index("expert")
    width = cols // len(orders)
    outs = []
    for s, order in enumerate(orders):
        part = term[:, :, s * width:(s + 1) * width].reshape([2] * n_bits + [rows, width])
        perm = [n_bits - 1 - b for b in order] + [n_bits, n_bits + 1]
        part = part.transpose(perm).reshape(n_exp, rows, width)
        for b in order:
            half = part.shape[0] // 2
            v = (me >> b) & 1
            keep = lax.dynamic_slice_in_dim(part, v * half, half, 0)
            send = lax.dynamic_slice_in_dim(part, (1 - v) * half, half, 0)
            part = keep + lax.ppermute(send, "expert", xor_pairs(n_exp, 1 << b))
        outs.append(part[0])
    return jnp.concatenate(outs, axis=-1)


def all_sum(x, order):
    n_exp = lax.axis_size("expert")
    for b in order:
        x = x + lax.ppermute(x, "expert", xor_pairs(n_exp, 1 << b))
    return x + lax.ppermute(x, "dp", [(0, 1), (1, 0)])


def bit_orders(n_exp, n_streams):
    n_bits = n_exp.bit_length() - 1
    if n_bits >= 5:
        axes = [[0, 1], [2, 3], list(range(4, n_bits))]
    else:
        axes = [list(range(n_bits))]
    orders = []
    for s in range(n_streams):
        turn = axes[s % len(axes):] + axes[:s % len(axes)]
        order = []
        for level in range(max(len(a) for a in turn)):
            order += [a[level] for a in turn if level < len(a)]
        orders.append(order)
    return orders


def local(hidden, routes, slots, down_weight, omega):
    n_exp = lax.axis_size("expert")
    n_dp = lax.axis_size("dp")
    tok_rows, n_route, hid_width = hidden.shape
    capacity = 2 * tok_rows * n_route // n_exp
    n_slot = n_exp * n_dp * capacity
    slot_index = (routes * capacity + slots).reshape(-1)
    outgoing = jnp.zeros((n_exp * capacity, hid_width), jnp.bfloat16)
    outgoing = (
        outgoing.at[slot_index]
        .set(hidden.reshape(-1, hid_width))
        .reshape(n_exp, capacity, hid_width)
    )
    received = lax.all_to_all(outgoing, "expert", split_axis=0, concat_axis=0, tiled=True).reshape(
        n_exp * capacity, hid_width
    )
    partner = lax.ppermute(received, "dp", [(0, 1), (1, 0)])
    gram_mat = (contract(received, received) + contract(partner, partner)) / n_slot
    on_diag = lax.broadcasted_iota(jnp.int32, gram_mat.shape, 0) == lax.broadcasted_iota(
        jnp.int32, gram_mat.shape, 1
    )
    diag_mean = jnp.sum(jnp.where(on_diag, gram_mat, 0.0)) / hid_width
    damped = jnp.where(on_diag, gram_mat + (damping * diag_mean + jitter), gram_mat)
    whitening = jnp.linalg.cholesky(damped)
    test_mat = jnp.dot(
        whitening, omega[0].astype(jnp.float32), precision=lax.Precision.HIGHEST
    ).astype(jnp.bfloat16)
    down_half = down_weight[0]
    half_cols = down_half.shape[1]
    term = contract(down_half, test_mat).reshape(n_exp, half_cols // n_exp, -1)
    orders = bit_orders(n_exp, 2)
    sketch = scatter_sum(term, orders)
    small_gram = all_sum(jnp.dot(sketch.T, sketch, precision=lax.Precision.HIGHEST), orders[0])
    qr_factor = jnp.linalg.cholesky(small_gram)
    basis_rows = jax.scipy.linalg.solve_triangular(qr_factor, sketch.T, lower=True).T * math.sqrt(
        half_cols * n_dp
    )
    own_rows = lax.dynamic_slice_in_dim(
        whitening, lax.axis_index("dp") * (hid_width // n_dp), hid_width // n_dp, 0
    )
    return (own_rows[None], basis_rows[None])


def solution(mesh):
    placed = (
        P(("expert", "dp"), None, None),
        P(("expert", "dp"), None),
        P(("expert", "dp"), None),
        P("expert", None, "dp"),
        P("expert", None, None),
    )
    return jax.shard_map(
        local,
        mesh=mesh,
        in_specs=placed,
        out_specs=(P("expert", "dp", None), P("dp", "expert", None)),
        check_vma=False,
    )
```

```python
import math

import jax
import jax.numpy as jnp
from jax import lax
from jax.sharding import PartitionSpec as P

damping = 0.1
jitter = 1e-06


def contract(left, right):
    return lax.dot_general(
        left, right, (((0,), (0,)), ((), ())), preferred_element_type=jnp.float32
    )


def torus_axes(n_exp):
    if n_exp == 128:
        return [(8, 16), (4, 4), (4, 1)]
    return [(n_exp, 1)]


def shift_pairs(n, size, stride, shift):
    pairs = []
    for i in range(n):
        p = (i // stride) % size
        pairs.append((i, i + ((p + shift) % size - p) * stride))
    return pairs


def to_axis_order(part, axes, order):
    sizes = [a[0] for a in axes]
    tail = list(part.shape[1:])
    part = part.reshape(sizes + tail)
    perm = list(order) + list(range(len(axes), len(axes) + len(tail)))
    return part.transpose(perm).reshape([-1] + tail)


def scatter_sum(term, orders):
    n_exp, rows, cols = term.shape
    axes = torus_axes(n_exp)
    me = lax.axis_index("expert")
    width = cols // len(orders)
    outs = []
    for s, order in enumerate(orders):
        part = to_axis_order(term[:, :, s * width:(s + 1) * width], axes, order)
        for a in order:
            size, stride = axes[a]
            p = (me // stride) % size
            chunk = part.shape[0] // size
            total = lax.dynamic_slice_in_dim(part, p * chunk, chunk, 0)
            for shift in range(1, size):
                send = lax.dynamic_slice_in_dim(part, ((p + shift) % size) * chunk, chunk, 0)
                total = total + lax.ppermute(
                    send, "expert", shift_pairs(n_exp, size, stride, shift)
                )
            part = total
        outs.append(part[0])
    return jnp.concatenate(outs, axis=-1)


def all_sum(x, orders):
    n_exp = lax.axis_size("expert")
    axes = torus_axes(n_exp)
    height = x.shape[0] // len(orders)
    outs = []
    for s, order in enumerate(orders):
        part = x[s * height:(s + 1) * height]
        for a in order:
            size, stride = axes[a]
            total = part
            for shift in range(1, size):
                total = total + lax.ppermute(
                    part, "expert", shift_pairs(n_exp, size, stride, shift)
                )
            part = total
        outs.append(part)
    x = jnp.concatenate(outs, axis=0)
    return x + lax.ppermute(x, "dp", [(0, 1), (1, 0)])


def axis_orders(n_exp):
    n_ax = len(torus_axes(n_exp))
    if n_ax == 3:
        return [(2, 1, 0), (1, 2, 0)]
    return [tuple(range(n_ax))] * 2


def local(hidden, routes, slots, down_weight, omega):
    n_exp = lax.axis_size("expert")
    n_dp = lax.axis_size("dp")
    tok_rows, n_route, hid_width = hidden.shape
    capacity = 2 * tok_rows * n_route // n_exp
    n_slot = n_exp * n_dp * capacity
    slot_index = (routes * capacity + slots).reshape(-1)
    outgoing = jnp.zeros((n_exp * capacity, hid_width), jnp.bfloat16)
    outgoing = (
        outgoing.at[slot_index]
        .set(hidden.reshape(-1, hid_width))
        .reshape(n_exp, capacity, hid_width)
    )
    received = lax.all_to_all(outgoing, "expert", split_axis=0, concat_axis=0, tiled=True).reshape(
        n_exp * capacity, hid_width
    )
    partner = lax.ppermute(received, "dp", [(0, 1), (1, 0)])
    gram_mat = (contract(received, received) + contract(partner, partner)) / n_slot
    on_diag = lax.broadcasted_iota(jnp.int32, gram_mat.shape, 0) == lax.broadcasted_iota(
        jnp.int32, gram_mat.shape, 1
    )
    diag_mean = jnp.sum(jnp.where(on_diag, gram_mat, 0.0)) / hid_width
    damped = jnp.where(on_diag, gram_mat + (damping * diag_mean + jitter), gram_mat)
    whitening = jnp.linalg.cholesky(damped)
    test_mat = jnp.dot(
        whitening, omega[0].astype(jnp.float32), precision=lax.Precision.HIGHEST
    ).astype(jnp.bfloat16)
    down_half = down_weight[0]
    half_cols = down_half.shape[1]
    term = contract(down_half, test_mat).reshape(n_exp, half_cols // n_exp, -1)
    orders = axis_orders(n_exp)
    sketch = scatter_sum(term, orders)
    small_gram = all_sum(jnp.dot(sketch.T, sketch, precision=lax.Precision.HIGHEST), orders)
    qr_factor = jnp.linalg.cholesky(small_gram)
    basis_rows = jax.scipy.linalg.solve_triangular(qr_factor, sketch.T, lower=True).T * math.sqrt(
        half_cols * n_dp
    )
    own_rows = lax.dynamic_slice_in_dim(
        whitening, lax.axis_index("dp") * (hid_width // n_dp), hid_width // n_dp, 0
    )
    return (own_rows[None], basis_rows[None])


def solution(mesh):
    placed = (
        P(("expert", "dp"), None, None),
        P(("expert", "dp"), None),
        P(("expert", "dp"), None),
        P("expert", None, "dp"),
        P("expert", None, None),
    )
    return jax.shard_map(
        local,
        mesh=mesh,
        in_specs=placed,
        out_specs=(P("expert", "dp", None), P("dp", "expert", None)),
        check_vma=False,
    )
```

```python
import functools
import math

import jax
import jax.numpy as jnp
from jax import lax
from jax.sharding import Mesh, PartitionSpec as P

damping = 0.1
jitter = 1e-06


def contract(left, right):
    return lax.dot_general(
        left, right, (((0,), (0,)), ((), ())), preferred_element_type=jnp.float32
    )


def torus_axes(n_exp):
    if n_exp == 128:
        return (("z", 8), ("x", 4), ("y", 4))
    return (("e", n_exp),)


def scatter_sum(term, orders, axes):
    n_exp, rows, cols = term.shape
    sizes = [size for _, size in axes]
    width = cols // len(orders)
    outs = []
    for s, order in enumerate(orders):
        part = term[:, :, s * width:(s + 1) * width].reshape(sizes + [rows, width])
        part = part.transpose(list(order) + [len(axes), len(axes) + 1])
        for a in order:
            name, size = axes[a]
            part = lax.all_to_all(part, name, 0, 0).sum(axis=0)
        outs.append(part.reshape(rows, width))
    return jnp.concatenate(outs, axis=-1)


def all_sum(x, orders, axes):
    height = x.shape[0] // len(orders)
    outs = []
    for s, order in enumerate(orders):
        part = x[s * height:(s + 1) * height]
        for a in order:
            name, size = axes[a]
            part = lax.all_to_all(jnp.broadcast_to(part, (size,) + part.shape), name, 0, 0).sum(axis=0)
        outs.append(part)
    x = jnp.concatenate(outs, axis=0)
    return x + lax.ppermute(x, "dp", [(0, 1), (1, 0)])


def axis_orders(n_ax):
    if n_ax == 3:
        return [(2, 1, 0), (1, 2, 0)]
    return [tuple(range(n_ax))] * 2


def local(hidden, routes, slots, down_weight, omega, axes):
    expert = tuple(name for name, _ in axes)
    n_exp = math.prod(size for _, size in axes)
    n_dp = lax.axis_size("dp")
    tok_rows, n_route, hid_width = hidden.shape
    capacity = 2 * tok_rows * n_route // n_exp
    n_slot = n_exp * n_dp * capacity
    slot_index = (routes * capacity + slots).reshape(-1)
    outgoing = jnp.zeros((n_exp * capacity, hid_width), jnp.bfloat16)
    outgoing = (
        outgoing.at[slot_index]
        .set(hidden.reshape(-1, hid_width))
        .reshape(n_exp, capacity, hid_width)
    )
    received = lax.all_to_all(outgoing, expert, split_axis=0, concat_axis=0, tiled=True).reshape(
        n_exp * capacity, hid_width
    )
    partner = lax.ppermute(received, "dp", [(0, 1), (1, 0)])
    gram_mat = (contract(received, received) + contract(partner, partner)) / n_slot
    on_diag = lax.broadcasted_iota(jnp.int32, gram_mat.shape, 0) == lax.broadcasted_iota(
        jnp.int32, gram_mat.shape, 1
    )
    diag_mean = jnp.sum(jnp.where(on_diag, gram_mat, 0.0)) / hid_width
    damped = jnp.where(on_diag, gram_mat + (damping * diag_mean + jitter), gram_mat)
    whitening = jnp.linalg.cholesky(damped)
    test_mat = jnp.dot(
        whitening, omega[0].astype(jnp.float32), precision=lax.Precision.HIGHEST
    ).astype(jnp.bfloat16)
    down_half = down_weight[0]
    half_cols = down_half.shape[1]
    term = contract(down_half, test_mat).reshape(n_exp, half_cols // n_exp, -1)
    orders = axis_orders(len(axes))
    sketch = scatter_sum(term, orders, axes)
    small_gram = all_sum(jnp.dot(sketch.T, sketch, precision=lax.Precision.HIGHEST), orders, axes)
    qr_factor = jnp.linalg.cholesky(small_gram)
    basis_rows = jax.scipy.linalg.solve_triangular(qr_factor, sketch.T, lower=True).T * math.sqrt(
        half_cols * n_dp
    )
    own_rows = lax.dynamic_slice_in_dim(
        whitening, lax.axis_index("dp") * (hid_width // n_dp), hid_width // n_dp, 0
    )
    return (own_rows[None], basis_rows[None])


def solution(mesh):
    n_exp = mesh.shape["expert"]
    axes = torus_axes(n_exp)
    names = tuple(name for name, _ in axes)
    grid = Mesh(mesh.devices.reshape([size for _, size in axes] + [mesh.shape["dp"]]), names + ("dp",))
    placed = (
        P(names + ("dp",), None, None),
        P(names + ("dp",), None),
        P(names + ("dp",), None),
        P(names, None, "dp"),
        P(names, None, None),
    )
    return jax.shard_map(
        functools.partial(local, axes=axes),
        mesh=grid,
        in_specs=placed,
        out_specs=(P(names, "dp", None), P("dp", names, None)),
        check_vma=False,
    )
```

```python
import math

import jax
import jax.numpy as jnp
from jax import lax
from jax.sharding import PartitionSpec as P

damping = 0.1
jitter = 1e-06


def contract(left, right):
    return lax.dot_general(
        left, right, (((0,), (0,)), ((), ())), preferred_element_type=jnp.float32
    )


def xor_pairs(n, mask):
    return [(i, i ^ mask) for i in range(n)]


def scatter_sum(term, orders):
    cols = term.shape[0]
    n_exp = lax.axis_size("expert")
    rows = term.shape[1] // n_exp
    n_bits = n_exp.bit_length() - 1
    me = lax.axis_index("expert")
    width = cols // len(orders)
    outs = []
    for s, order in enumerate(orders):
        part = term[s * width:(s + 1) * width].reshape([width] + [2] * n_bits + [rows])
        perm = [n_bits - b for b in order] + [n_bits + 1, 0]
        part = part.transpose(perm).reshape(n_exp, rows, width)
        for b in order:
            half = part.shape[0] // 2
            v = (me >> b) & 1
            keep = lax.dynamic_slice_in_dim(part, v * half, half, 0)
            send = lax.dynamic_slice_in_dim(part, (1 - v) * half, half, 0)
            part = keep + lax.ppermute(send, "expert", xor_pairs(n_exp, 1 << b))
        outs.append(part[0])
    return jnp.concatenate(outs, axis=-1)


def all_sum(x, order):
    n_exp = lax.axis_size("expert")
    for b in order:
        x = x + lax.ppermute(x, "expert", xor_pairs(n_exp, 1 << b))
    return x + lax.ppermute(x, "dp", [(0, 1), (1, 0)])


def bit_orders(n_exp, n_streams):
    n_bits = n_exp.bit_length() - 1
    if n_bits >= 5:
        axes = [[0, 1], [2, 3], list(range(4, n_bits))]
    else:
        axes = [list(range(n_bits))]
    orders = []
    for s in range(n_streams):
        turn = axes[s % len(axes):] + axes[:s % len(axes)]
        order = []
        for level in range(max(len(a) for a in turn)):
            order += [a[level] for a in turn if level < len(a)]
        orders.append(order)
    return orders


def local(hidden, routes, slots, down_weight, omega):
    n_exp = lax.axis_size("expert")
    n_dp = lax.axis_size("dp")
    tok_rows, n_route, hid_width = hidden.shape
    capacity = 2 * tok_rows * n_route // n_exp
    n_slot = n_exp * n_dp * capacity
    slot_index = (routes * capacity + slots).reshape(-1)
    outgoing = jnp.zeros((n_exp * capacity, hid_width), jnp.bfloat16)
    outgoing = (
        outgoing.at[slot_index]
        .set(hidden.reshape(-1, hid_width))
        .reshape(n_exp, capacity, hid_width)
    )
    received = lax.all_to_all(outgoing, "expert", split_axis=0, concat_axis=0, tiled=True).reshape(
        n_exp * capacity, hid_width
    )
    partner = lax.ppermute(received, "dp", [(0, 1), (1, 0)])
    gram_mat = (contract(received, received) + contract(partner, partner)) / n_slot
    on_diag = lax.broadcasted_iota(jnp.int32, gram_mat.shape, 0) == lax.broadcasted_iota(
        jnp.int32, gram_mat.shape, 1
    )
    diag_mean = jnp.sum(jnp.where(on_diag, gram_mat, 0.0)) / hid_width
    damped = jnp.where(on_diag, gram_mat + (damping * diag_mean + jitter), gram_mat)
    whitening = jnp.linalg.cholesky(damped, symmetrize_input=False)
    test_mat = jnp.dot(
        whitening, omega[0].astype(jnp.float32), precision=lax.Precision.HIGHEST
    ).astype(jnp.bfloat16)
    down_half = down_weight[0]
    half_cols = down_half.shape[1]
    term = contract(test_mat, down_half)
    orders = bit_orders(n_exp, 2)
    sketch = scatter_sum(term, orders)
    small_gram = all_sum(jnp.dot(sketch.T, sketch, precision=lax.Precision.HIGHEST), orders[0])
    qr_factor = jnp.linalg.cholesky(small_gram, symmetrize_input=False)
    basis_rows = jax.scipy.linalg.solve_triangular(qr_factor, sketch.T, lower=True).T * math.sqrt(
        half_cols * n_dp
    )
    own_rows = lax.dynamic_slice_in_dim(
        whitening, lax.axis_index("dp") * (hid_width // n_dp), hid_width // n_dp, 0
    )
    return (own_rows[None], basis_rows[None])


def solution(mesh):
    placed = (
        P(("expert", "dp"), None, None),
        P(("expert", "dp"), None),
        P(("expert", "dp"), None),
        P("expert", None, "dp"),
        P("expert", None, None),
    )
    return jax.shard_map(
        local,
        mesh=mesh,
        in_specs=placed,
        out_specs=(P("expert", "dp", None), P("dp", "expert", None)),
        check_vma=False,
    )
```

```python
import math

import jax
import jax.numpy as jnp
from jax import lax
from jax.sharding import PartitionSpec as P

damping = 0.1
jitter = 1e-06


def contract(left, right):
    return lax.dot_general(
        left, right, (((0,), (0,)), ((), ())), preferred_element_type=jnp.float32
    )


def xor_pairs(n, mask):
    return [(i, i ^ mask) for i in range(n)]


def scatter_sum(term, orders):
    cols = term.shape[0]
    n_exp = lax.axis_size("expert")
    rows = term.shape[1] // n_exp
    n_bits = n_exp.bit_length() - 1
    me = lax.axis_index("expert")
    width = cols // len(orders)
    outs = []
    for s, order in enumerate(orders):
        part = term[s * width:(s + 1) * width].reshape([width] + [2] * n_bits + [rows])
        perm = [n_bits - b for b in order] + [n_bits + 1, 0]
        part = part.transpose(perm).reshape(n_exp, rows, width)
        for b in order:
            half = part.shape[0] // 2
            v = (me >> b) & 1
            keep = lax.dynamic_slice_in_dim(part, v * half, half, 0)
            send = lax.dynamic_slice_in_dim(part, (1 - v) * half, half, 0)
            part = keep + lax.ppermute(send, "expert", xor_pairs(n_exp, 1 << b))
        outs.append(part[0])
    return jnp.concatenate(outs, axis=-1)


def all_sum(x, order):
    n_exp = lax.axis_size("expert")
    for b in order:
        x = x + lax.ppermute(x, "expert", xor_pairs(n_exp, 1 << b))
    return x + lax.ppermute(x, "dp", [(0, 1), (1, 0)])


def bit_orders(n_exp, n_streams):
    n_bits = n_exp.bit_length() - 1
    if n_bits >= 5:
        axes = [[0, 1], [2, 3], list(range(4, n_bits))]
    else:
        axes = [list(range(n_bits))]
    orders = []
    for s in range(n_streams):
        turn = axes[s % len(axes):] + axes[:s % len(axes)]
        order = []
        for level in range(max(len(a) for a in turn)):
            order += [a[level] for a in turn if level < len(a)]
        orders.append(order)
    return orders


def hdot(left, right):
    return jnp.dot(left, right, precision=lax.Precision.HIGHEST)


def right_solve_chol(gram, rows):
    h = gram.shape[0] // 2
    eye = jnp.eye(h, dtype=gram.dtype)
    l11 = jnp.linalg.cholesky(gram[:h, :h], symmetrize_input=False)
    i11 = jax.scipy.linalg.solve_triangular(l11, eye, lower=True)
    l21 = hdot(gram[h:, :h], i11.T)
    l22 = jnp.linalg.cholesky(gram[h:, h:] - hdot(l21, l21.T), symmetrize_input=False)
    i22 = jax.scipy.linalg.solve_triangular(l22, eye, lower=True)
    x1 = hdot(rows[:, :h], i11.T)
    x2 = hdot(rows[:, h:] - hdot(x1, l21.T), i22.T)
    return jnp.concatenate([x1, x2], axis=1)


def local(hidden, routes, slots, down_weight, omega):
    n_exp = lax.axis_size("expert")
    n_dp = lax.axis_size("dp")
    tok_rows, n_route, hid_width = hidden.shape
    capacity = 2 * tok_rows * n_route // n_exp
    n_slot = n_exp * n_dp * capacity
    slot_index = (routes * capacity + slots).reshape(-1)
    outgoing = jnp.zeros((n_exp * capacity, hid_width), jnp.bfloat16)
    outgoing = (
        outgoing.at[slot_index]
        .set(hidden.reshape(-1, hid_width))
        .reshape(n_exp, capacity, hid_width)
    )
    received = lax.all_to_all(outgoing, "expert", split_axis=0, concat_axis=0, tiled=True).reshape(
        n_exp * capacity, hid_width
    )
    partner = lax.ppermute(received, "dp", [(0, 1), (1, 0)])
    gram_mat = (contract(received, received) + contract(partner, partner)) / n_slot
    on_diag = lax.broadcasted_iota(jnp.int32, gram_mat.shape, 0) == lax.broadcasted_iota(
        jnp.int32, gram_mat.shape, 1
    )
    diag_mean = jnp.sum(jnp.where(on_diag, gram_mat, 0.0)) / hid_width
    damped = jnp.where(on_diag, gram_mat + (damping * diag_mean + jitter), gram_mat)
    whitening = jnp.linalg.cholesky(damped, symmetrize_input=False)
    test_mat = jnp.dot(
        whitening, omega[0].astype(jnp.float32), precision=lax.Precision.HIGHEST
    ).astype(jnp.bfloat16)
    down_half = down_weight[0]
    half_cols = down_half.shape[1]
    term = contract(test_mat, down_half)
    orders = bit_orders(n_exp, 2)
    sketch = scatter_sum(term, orders)
    small_gram = all_sum(jnp.dot(sketch.T, sketch, precision=lax.Precision.HIGHEST), orders[0])
    basis_rows = right_solve_chol(small_gram, sketch) * math.sqrt(half_cols * n_dp)
    own_rows = lax.dynamic_slice_in_dim(
        whitening, lax.axis_index("dp") * (hid_width // n_dp), hid_width // n_dp, 0
    )
    return (own_rows[None], basis_rows[None])


def solution(mesh):
    placed = (
        P(("expert", "dp"), None, None),
        P(("expert", "dp"), None),
        P(("expert", "dp"), None),
        P("expert", None, "dp"),
        P("expert", None, None),
    )
    return jax.shard_map(
        local,
        mesh=mesh,
        in_specs=placed,
        out_specs=(P("expert", "dp", None), P("dp", "expert", None)),
        check_vma=False,
    )
```

```python
import math

import jax
import jax.numpy as jnp
from jax import lax
from jax.sharding import PartitionSpec as P

damping = 0.1
jitter = 1e-06


def contract(left, right):
    return lax.dot_general(
        left, right, (((0,), (0,)), ((), ())), preferred_element_type=jnp.float32
    )


def xor_pairs(n, mask):
    return [(i, i ^ mask) for i in range(n)]


def scatter_sum(term, orders):
    cols = term.shape[0]
    n_exp = lax.axis_size("expert")
    rows = term.shape[1] // n_exp
    n_bits = n_exp.bit_length() - 1
    me = lax.axis_index("expert")
    width = cols // len(orders)
    outs = []
    for s, order in enumerate(orders):
        part = term[s * width:(s + 1) * width].reshape([width] + [2] * n_bits + [rows])
        perm = [n_bits - b for b in order] + [n_bits + 1, 0]
        part = part.transpose(perm).reshape(n_exp, rows, width)
        for b in order:
            half = part.shape[0] // 2
            v = (me >> b) & 1
            keep = lax.dynamic_slice_in_dim(part, v * half, half, 0)
            send = lax.dynamic_slice_in_dim(part, (1 - v) * half, half, 0)
            part = keep + lax.ppermute(send, "expert", xor_pairs(n_exp, 1 << b))
        outs.append(part[0])
    return jnp.concatenate(outs, axis=-1)


def all_sum(x, order):
    n_exp = lax.axis_size("expert")
    for b in order:
        x = x + lax.ppermute(x, "expert", xor_pairs(n_exp, 1 << b))
    return x + lax.ppermute(x, "dp", [(0, 1), (1, 0)])


def bit_orders(n_exp, n_streams):
    n_bits = n_exp.bit_length() - 1
    if n_bits >= 5:
        axes = [[0, 1], [2, 3], list(range(4, n_bits))]
    else:
        axes = [list(range(n_bits))]
    orders = []
    for s in range(n_streams):
        turn = axes[s % len(axes):] + axes[:s % len(axes)]
        order = []
        for level in range(max(len(a) for a in turn)):
            order += [a[level] for a in turn if level < len(a)]
        orders.append(order)
    return orders


def hdot(left, right):
    return jnp.dot(left, right, precision=lax.Precision.HIGHEST)


def lower_blocks(rows):
    h = rows.shape[1] // 2
    left, right = rows[:, :h], rows[:, h:]
    return jnp.concatenate([hdot(left.T, left), hdot(right.T, left), hdot(right.T, right)], axis=0)


def right_solve_chol(blocks, rows):
    h = blocks.shape[1]
    eye = jnp.eye(h, dtype=blocks.dtype)
    l11 = jnp.linalg.cholesky(blocks[:h], symmetrize_input=False)
    i11 = jax.scipy.linalg.solve_triangular(l11, eye, lower=True)
    l21 = hdot(blocks[h:2 * h], i11.T)
    l22 = jnp.linalg.cholesky(blocks[2 * h:] - hdot(l21, l21.T), symmetrize_input=False)
    i22 = jax.scipy.linalg.solve_triangular(l22, eye, lower=True)
    x1 = hdot(rows[:, :h], i11.T)
    x2 = hdot(rows[:, h:] - hdot(x1, l21.T), i22.T)
    return jnp.concatenate([x1, x2], axis=1)


def local(hidden, routes, slots, down_weight, omega):
    n_exp = lax.axis_size("expert")
    n_dp = lax.axis_size("dp")
    tok_rows, n_route, hid_width = hidden.shape
    capacity = 2 * tok_rows * n_route // n_exp
    n_slot = n_exp * n_dp * capacity
    slot_index = (routes * capacity + slots).reshape(-1)
    one_hot = (
        slot_index[:, None] == lax.broadcasted_iota(jnp.int32, (1, n_exp * capacity), 1)
    ).astype(jnp.bfloat16)
    outgoing = contract(one_hot, hidden.reshape(-1, hid_width)).astype(jnp.bfloat16)
    outgoing = outgoing.reshape(n_exp, capacity, hid_width)
    received = lax.all_to_all(outgoing, "expert", split_axis=0, concat_axis=0, tiled=True).reshape(
        n_exp * capacity, hid_width
    )
    partner = lax.ppermute(received, "dp", [(0, 1), (1, 0)])
    gram_mat = (contract(received, received) + contract(partner, partner)) / n_slot
    on_diag = lax.broadcasted_iota(jnp.int32, gram_mat.shape, 0) == lax.broadcasted_iota(
        jnp.int32, gram_mat.shape, 1
    )
    diag_mean = jnp.sum(jnp.where(on_diag, gram_mat, 0.0)) / hid_width
    damped = jnp.where(on_diag, gram_mat + (damping * diag_mean + jitter), gram_mat)
    whitening = jnp.linalg.cholesky(damped, symmetrize_input=False)
    test_mat = jnp.dot(
        whitening, omega[0].astype(jnp.float32), precision=lax.Precision.HIGHEST
    ).astype(jnp.bfloat16)
    down_half = down_weight[0]
    half_cols = down_half.shape[1]
    term = contract(test_mat, down_half)
    orders = bit_orders(n_exp, 2)
    sketch = scatter_sum(term, orders)
    small_gram = all_sum(lower_blocks(sketch), orders[0])
    basis_rows = right_solve_chol(small_gram, sketch) * math.sqrt(half_cols * n_dp)
    own_rows = lax.dynamic_slice_in_dim(
        whitening, lax.axis_index("dp") * (hid_width // n_dp), hid_width // n_dp, 0
    )
    return (own_rows[None], basis_rows[None])


def solution(mesh):
    placed = (
        P(("expert", "dp"), None, None),
        P(("expert", "dp"), None),
        P(("expert", "dp"), None),
        P("expert", None, "dp"),
        P("expert", None, None),
    )
    return jax.shard_map(
        local,
        mesh=mesh,
        in_specs=placed,
        out_specs=(P("expert", "dp", None), P("dp", "expert", None)),
        check_vma=False,
    )
```

```python
import math

import jax
import jax.numpy as jnp
from jax import lax
from jax.sharding import PartitionSpec as P

damping = 0.1
jitter = 1e-06


def contract(left, right):
    return lax.dot_general(
        left, right, (((0,), (0,)), ((), ())), preferred_element_type=jnp.float32
    )


def xor_pairs(n, mask):
    return [(i, i ^ mask) for i in range(n)]


def scatter_sum(term, orders):
    cols = term.shape[0]
    n_exp = lax.axis_size("expert")
    rows = term.shape[1] // n_exp
    n_bits = n_exp.bit_length() - 1
    me = lax.axis_index("expert")
    width = cols // len(orders)
    outs = []
    def halve(part, b):
        half = part.shape[0] // 2
        v = (me >> b) & 1
        keep = lax.dynamic_slice_in_dim(part, v * half, half, 0)
        send = lax.dynamic_slice_in_dim(part, (1 - v) * half, half, 0)
        return keep + lax.ppermute(send, "expert", xor_pairs(n_exp, 1 << b))

    lead = next(k for k in range(n_bits + 1) if all(o[k:] == orders[0][k:] for o in orders))
    for s, order in enumerate(orders):
        part = term[s * width:(s + 1) * width].reshape([width] + [2] * n_bits + [rows])
        perm = [n_bits - b for b in order] + [n_bits + 1, 0]
        part = part.transpose(perm).reshape(n_exp, rows, width)
        for b in order[:lead]:
            part = halve(part, b)
        outs.append(part)
    part = jnp.concatenate(outs, axis=-1)
    for b in orders[0][lead:]:
        part = halve(part, b)
    return part[0]


def all_sum(x, order):
    n_exp = lax.axis_size("expert")
    for b in order:
        x = x + lax.ppermute(x, "expert", xor_pairs(n_exp, 1 << b))
    return x + lax.ppermute(x, "dp", [(0, 1), (1, 0)])


def bit_orders(n_exp, n_streams):
    n_bits = n_exp.bit_length() - 1
    if n_bits >= 5:
        axes = [[0, 1], [2, 3], list(range(4, n_bits))]
    else:
        axes = [list(range(n_bits))]
    orders = []
    for s in range(n_streams):
        turn = axes[s % len(axes):] + axes[:s % len(axes)]
        order = [a[0] for a in turn]
        for level in range(1, max(len(a) for a in axes)):
            order += [a[level] for a in axes if level < len(a)]
        orders.append(order)
    return orders


def hdot(left, right):
    return jnp.dot(left, right, precision=lax.Precision.HIGHEST)


def lower_blocks(rows):
    h = rows.shape[1] // 2
    left, right = rows[:, :h], rows[:, h:]
    return jnp.concatenate([hdot(left.T, left), hdot(right.T, left), hdot(right.T, right)], axis=0)


def right_solve_chol(blocks, rows):
    h = blocks.shape[1]
    eye = jnp.eye(h, dtype=blocks.dtype)
    l11 = jnp.linalg.cholesky(blocks[:h], symmetrize_input=False)
    i11 = jax.scipy.linalg.solve_triangular(l11, eye, lower=True)
    l21 = hdot(blocks[h:2 * h], i11.T)
    l22 = jnp.linalg.cholesky(blocks[2 * h:] - hdot(l21, l21.T), symmetrize_input=False)
    i22 = jax.scipy.linalg.solve_triangular(l22, eye, lower=True)
    x1 = hdot(rows[:, :h], i11.T)
    x2 = hdot(rows[:, h:] - hdot(x1, l21.T), i22.T)
    return jnp.concatenate([x1, x2], axis=1)


def local(hidden, routes, slots, down_weight, omega):
    n_exp = lax.axis_size("expert")
    n_dp = lax.axis_size("dp")
    tok_rows, n_route, hid_width = hidden.shape
    capacity = 2 * tok_rows * n_route // n_exp
    n_slot = n_exp * n_dp * capacity
    slot_index = (routes * capacity + slots).reshape(-1)
    one_hot = (
        slot_index[:, None] == lax.broadcasted_iota(jnp.int32, (1, n_exp * capacity), 1)
    ).astype(jnp.bfloat16)
    outgoing = contract(one_hot, hidden.reshape(-1, hid_width)).astype(jnp.bfloat16)
    outgoing = outgoing.reshape(n_exp, capacity, hid_width)
    received = lax.all_to_all(outgoing, "expert", split_axis=0, concat_axis=0, tiled=True).reshape(
        n_exp * capacity, hid_width
    )
    partner = lax.ppermute(received, "dp", [(0, 1), (1, 0)])
    gram_mat = (contract(received, received) + contract(partner, partner)) / n_slot
    on_diag = lax.broadcasted_iota(jnp.int32, gram_mat.shape, 0) == lax.broadcasted_iota(
        jnp.int32, gram_mat.shape, 1
    )
    diag_mean = jnp.sum(jnp.where(on_diag, gram_mat, 0.0)) / hid_width
    damped = jnp.where(on_diag, gram_mat + (damping * diag_mean + jitter), gram_mat)
    whitening = jnp.linalg.cholesky(damped, symmetrize_input=False)
    test_mat = jnp.dot(
        whitening, omega[0].astype(jnp.float32), precision=lax.Precision.HIGHEST
    ).astype(jnp.bfloat16)
    down_half = down_weight[0]
    half_cols = down_half.shape[1]
    term = contract(test_mat, down_half)
    orders = bit_orders(n_exp, 2)
    sketch = scatter_sum(term, orders)
    small_gram = all_sum(lower_blocks(sketch), orders[0])
    basis_rows = right_solve_chol(small_gram, sketch) * math.sqrt(half_cols * n_dp)
    own_rows = lax.dynamic_slice_in_dim(
        whitening, lax.axis_index("dp") * (hid_width // n_dp), hid_width // n_dp, 0
    )
    return (own_rows[None], basis_rows[None])


def solution(mesh):
    placed = (
        P(("expert", "dp"), None, None),
        P(("expert", "dp"), None),
        P(("expert", "dp"), None),
        P("expert", None, "dp"),
        P("expert", None, None),
    )
    return jax.shard_map(
        local,
        mesh=mesh,
        in_specs=placed,
        out_specs=(P("expert", "dp", None), P("dp", "expert", None)),
        check_vma=False,
    )
```

```python
import math

import jax
import jax.numpy as jnp
from jax import lax
from jax.sharding import PartitionSpec as P

damping = 0.1
jitter = 1e-06


def contract(left, right):
    return lax.dot_general(
        left, right, (((0,), (0,)), ((), ())), preferred_element_type=jnp.float32
    )


def xor_pairs(n, mask):
    return [(i, i ^ mask) for i in range(n)]


def scatter_sum(term, orders):
    cols = term.shape[0]
    n_exp = lax.axis_size("expert")
    rows = term.shape[1] // n_exp
    n_bits = n_exp.bit_length() - 1
    me = lax.axis_index("expert")
    width = cols // len(orders)
    outs = []
    for s, order in enumerate(orders):
        part = term[s * width:(s + 1) * width].reshape([width] + [2] * n_bits + [rows])
        perm = [n_bits - b for b in order] + [n_bits + 1, 0]
        part = part.transpose(perm).reshape(n_exp, rows, width)
        for b in order:
            half = part.shape[0] // 2
            v = (me >> b) & 1
            keep = lax.dynamic_slice_in_dim(part, v * half, half, 0)
            send = lax.dynamic_slice_in_dim(part, (1 - v) * half, half, 0)
            part = keep + lax.ppermute(send, "expert", xor_pairs(n_exp, 1 << b))
        outs.append(part[0])
    return jnp.concatenate(outs, axis=-1)


def all_sum(x, order):
    n_exp = lax.axis_size("expert")
    for b in order:
        x = x + lax.ppermute(x, "expert", xor_pairs(n_exp, 1 << b))
    return x + lax.ppermute(x, "dp", [(0, 1), (1, 0)])


def bit_orders(n_exp, n_streams):
    n_bits = n_exp.bit_length() - 1
    if n_bits >= 5:
        axes = [[0, 1], [2, 3], list(range(4, n_bits))]
    else:
        axes = [list(range(n_bits))]
    orders = []
    for s in range(n_streams):
        turn = axes[s % len(axes):] + axes[:s % len(axes)]
        order = []
        for level in range(max(len(a) for a in turn)):
            order += [a[level] for a in turn if level < len(a)]
        orders.append(order)
    return orders


def hdot(left, right):
    return jnp.dot(left, right, precision=lax.Precision.HIGHEST)


def lower_blocks(rows):
    h = rows.shape[1] // 2
    left, right = rows[:, :h], rows[:, h:]
    return jnp.concatenate([hdot(left.T, left), hdot(right.T, left), hdot(right.T, right)], axis=0)


def right_solve_chol(blocks, rows):
    h = blocks.shape[1]
    eye = jnp.eye(h, dtype=blocks.dtype)
    l11 = jnp.linalg.cholesky(blocks[:h], symmetrize_input=False)
    i11 = jax.scipy.linalg.solve_triangular(l11, eye, lower=True)
    l21 = hdot(blocks[h:2 * h], i11.T)
    l22 = jnp.linalg.cholesky(blocks[2 * h:] - hdot(l21, l21.T), symmetrize_input=False)
    i22 = jax.scipy.linalg.solve_triangular(l22, eye, lower=True)
    x1 = hdot(rows[:, :h], i11.T)
    x2 = hdot(rows[:, h:] - hdot(x1, l21.T), i22.T)
    return jnp.concatenate([x1, x2], axis=1)


def local(hidden, routes, slots, down_weight, omega):
    n_exp = lax.axis_size("expert")
    n_dp = lax.axis_size("dp")
    tok_rows, n_route, hid_width = hidden.shape
    capacity = 2 * tok_rows * n_route // n_exp
    n_slot = n_exp * n_dp * capacity
    slot_index = (routes * capacity + slots).reshape(-1)
    one_hot = (
        slot_index[:, None] == lax.broadcasted_iota(jnp.int32, (1, n_exp * capacity), 1)
    ).astype(jnp.bfloat16)
    outgoing = contract(one_hot, hidden.reshape(-1, hid_width)).astype(jnp.bfloat16)
    outgoing = outgoing.reshape(n_exp, capacity, hid_width)
    received = lax.all_to_all(outgoing, "expert", split_axis=0, concat_axis=0, tiled=True).reshape(
        n_exp * capacity, hid_width
    )
    partner = lax.ppermute(received, "dp", [(0, 1), (1, 0)])
    half_w = hid_width // 2

    def block(i, j):
        ri = slice(i * half_w, (i + 1) * half_w)
        rj = slice(j * half_w, (j + 1) * half_w)
        return contract(received[:, ri], received[:, rj]) + contract(partner[:, ri], partner[:, rj])

    g11, g21, g22 = block(0, 0), block(1, 0), block(1, 1)
    gram_mat = jnp.concatenate(
        [jnp.concatenate([g11, g21.T], axis=1), jnp.concatenate([g21, g22], axis=1)], axis=0
    ) / n_slot
    on_diag = lax.broadcasted_iota(jnp.int32, gram_mat.shape, 0) == lax.broadcasted_iota(
        jnp.int32, gram_mat.shape, 1
    )
    diag_mean = jnp.sum(jnp.where(on_diag, gram_mat, 0.0)) / hid_width
    damped = jnp.where(on_diag, gram_mat + (damping * diag_mean + jitter), gram_mat)
    whitening = jnp.linalg.cholesky(damped, symmetrize_input=False)
    test_mat = jnp.dot(
        whitening, omega[0].astype(jnp.float32), precision=lax.Precision.HIGHEST
    ).astype(jnp.bfloat16)
    down_half = down_weight[0]
    half_cols = down_half.shape[1]
    term = contract(test_mat, down_half)
    orders = bit_orders(n_exp, 2)
    sketch = scatter_sum(term, orders)
    small_gram = all_sum(lower_blocks(sketch), orders[0])
    basis_rows = right_solve_chol(small_gram, sketch) * math.sqrt(half_cols * n_dp)
    own_rows = lax.dynamic_slice_in_dim(
        whitening, lax.axis_index("dp") * (hid_width // n_dp), hid_width // n_dp, 0
    )
    return (own_rows[None], basis_rows[None])


def solution(mesh):
    placed = (
        P(("expert", "dp"), None, None),
        P(("expert", "dp"), None),
        P(("expert", "dp"), None),
        P("expert", None, "dp"),
        P("expert", None, None),
    )
    return jax.shard_map(
        local,
        mesh=mesh,
        in_specs=placed,
        out_specs=(P("expert", "dp", None), P("dp", "expert", None)),
        check_vma=False,
    )
```

```python
import math

import jax
import jax.numpy as jnp
from jax import lax
from jax.sharding import PartitionSpec as P

damping = 0.1
jitter = 1e-06


def contract(left, right):
    return lax.dot_general(
        left, right, (((0,), (0,)), ((), ())), preferred_element_type=jnp.float32
    )


def xor_pairs(n, mask):
    return [(i, i ^ mask) for i in range(n)]


def scatter_sum(term, n_cols, n_rows, orders):
    cols, n_exp = n_cols, lax.axis_size("expert")
    rows = n_rows // n_exp
    n_bits = n_exp.bit_length() - 1
    me = lax.axis_index("expert")
    width = cols // len(orders)
    outs = []
    for s, order in enumerate(orders):
        part = term(s * width, width).reshape([width] + [2] * n_bits + [rows])
        perm = [n_bits - b for b in order] + [n_bits + 1, 0]
        part = part.transpose(perm).reshape(n_exp, rows, width)
        for b in order:
            half = part.shape[0] // 2
            v = (me >> b) & 1
            keep = lax.dynamic_slice_in_dim(part, v * half, half, 0)
            send = lax.dynamic_slice_in_dim(part, (1 - v) * half, half, 0)
            part = keep + lax.ppermute(send, "expert", xor_pairs(n_exp, 1 << b))
        outs.append(part[0])
    return jnp.concatenate(outs, axis=-1)


def all_sum(x, order):
    n_exp = lax.axis_size("expert")
    for b in order:
        x = x + lax.ppermute(x, "expert", xor_pairs(n_exp, 1 << b))
    return x + lax.ppermute(x, "dp", [(0, 1), (1, 0)])


def bit_orders(n_exp, n_streams):
    n_bits = n_exp.bit_length() - 1
    if n_bits >= 5:
        axes = [[0, 1], [2, 3], list(range(4, n_bits))]
    else:
        axes = [list(range(n_bits))]
    orders = []
    for s in range(n_streams):
        turn = axes[s % len(axes):] + axes[:s % len(axes)]
        order = []
        for level in range(max(len(a) for a in turn)):
            order += [a[level] for a in turn if level < len(a)]
        orders.append(order)
    return orders


def hdot(left, right):
    return jnp.dot(left, right, precision=lax.Precision.HIGHEST)


def lower_blocks(rows):
    h = rows.shape[1] // 2
    left, right = rows[:, :h], rows[:, h:]
    return jnp.concatenate([hdot(left.T, left), hdot(right.T, left), hdot(right.T, right)], axis=0)


def right_solve_chol(blocks, rows):
    h = blocks.shape[1]
    eye = jnp.eye(h, dtype=blocks.dtype)
    l11 = jnp.linalg.cholesky(blocks[:h], symmetrize_input=False)
    i11 = jax.scipy.linalg.solve_triangular(l11, eye, lower=True)
    l21 = hdot(blocks[h:2 * h], i11.T)
    l22 = jnp.linalg.cholesky(blocks[2 * h:] - hdot(l21, l21.T), symmetrize_input=False)
    i22 = jax.scipy.linalg.solve_triangular(l22, eye, lower=True)
    x1 = hdot(rows[:, :h], i11.T)
    x2 = hdot(rows[:, h:] - hdot(x1, l21.T), i22.T)
    return jnp.concatenate([x1, x2], axis=1)


def local(hidden, routes, slots, down_weight, omega):
    n_exp = lax.axis_size("expert")
    n_dp = lax.axis_size("dp")
    tok_rows, n_route, hid_width = hidden.shape
    capacity = 2 * tok_rows * n_route // n_exp
    n_slot = n_exp * n_dp * capacity
    slot_index = (routes * capacity + slots).reshape(-1)
    one_hot = (
        slot_index[:, None] == lax.broadcasted_iota(jnp.int32, (1, n_exp * capacity), 1)
    ).astype(jnp.bfloat16)
    outgoing = contract(one_hot, hidden.reshape(-1, hid_width)).astype(jnp.bfloat16)
    outgoing = outgoing.reshape(n_exp, capacity, hid_width)
    received = lax.all_to_all(outgoing, "expert", split_axis=0, concat_axis=0, tiled=True).reshape(
        n_exp * capacity, hid_width
    )
    partner = lax.ppermute(received, "dp", [(0, 1), (1, 0)])
    gram_mat = (contract(received, received) + contract(partner, partner)) / n_slot
    on_diag = lax.broadcasted_iota(jnp.int32, gram_mat.shape, 0) == lax.broadcasted_iota(
        jnp.int32, gram_mat.shape, 1
    )
    diag_mean = jnp.sum(jnp.where(on_diag, gram_mat, 0.0)) / hid_width
    damped = jnp.where(on_diag, gram_mat + (damping * diag_mean + jitter), gram_mat)
    whitening = jnp.linalg.cholesky(damped, symmetrize_input=False)
    test_mat = jnp.dot(
        whitening, omega[0].astype(jnp.float32), precision=lax.Precision.HIGHEST
    ).astype(jnp.bfloat16)
    down_half = down_weight[0]
    half_cols = down_half.shape[1]
    def term(start, width):
        return contract(test_mat[:, start:start + width], down_half)

    orders = bit_orders(n_exp, 2)
    sketch = scatter_sum(term, test_mat.shape[1], half_cols, orders)
    small_gram = all_sum(lower_blocks(sketch), orders[0])
    basis_rows = right_solve_chol(small_gram, sketch) * math.sqrt(half_cols * n_dp)
    own_rows = lax.dynamic_slice_in_dim(
        whitening, lax.axis_index("dp") * (hid_width // n_dp), hid_width // n_dp, 0
    )
    return (own_rows[None], basis_rows[None])


def solution(mesh):
    placed = (
        P(("expert", "dp"), None, None),
        P(("expert", "dp"), None),
        P(("expert", "dp"), None),
        P("expert", None, "dp"),
        P("expert", None, None),
    )
    return jax.shard_map(
        local,
        mesh=mesh,
        in_specs=placed,
        out_specs=(P("expert", "dp", None), P("dp", "expert", None)),
        check_vma=False,
    )
```

```python
import math

import jax
import jax.numpy as jnp
from jax import lax
from jax.sharding import PartitionSpec as P

damping = 0.1
jitter = 1e-06


def contract(left, right):
    return lax.dot_general(
        left, right, (((0,), (0,)), ((), ())), preferred_element_type=jnp.float32
    )


def xor_pairs(n, mask):
    return [(i, i ^ mask) for i in range(n)]


def scatter_sum(term, n_cols, n_rows, orders):
    cols, n_exp = n_cols, lax.axis_size("expert")
    rows = n_rows // n_exp
    n_bits = n_exp.bit_length() - 1
    me = lax.axis_index("expert")
    width = cols // len(orders)
    outs = []
    for s, order in enumerate(orders):
        part = term(s * width, width).reshape([width] + [2] * n_bits + [rows])
        perm = [n_bits - b for b in order] + [n_bits + 1, 0]
        part = part.transpose(perm).reshape(n_exp, rows, width)
        for b in order:
            half = part.shape[0] // 2
            v = (me >> b) & 1
            keep = lax.dynamic_slice_in_dim(part, v * half, half, 0)
            send = lax.dynamic_slice_in_dim(part, (1 - v) * half, half, 0)
            part = keep + lax.ppermute(send, "expert", xor_pairs(n_exp, 1 << b))
        outs.append(part[0])
    return jnp.concatenate(outs, axis=-1)


def all_sum(x, order):
    n_exp = lax.axis_size("expert")
    for b in order:
        x = x + lax.ppermute(x, "expert", xor_pairs(n_exp, 1 << b))
    return x + lax.ppermute(x, "dp", [(0, 1), (1, 0)])


def bit_orders(n_exp, n_streams):
    n_bits = n_exp.bit_length() - 1
    if n_bits >= 5:
        axes = [[0, 1], [2, 3], list(range(4, n_bits))]
    else:
        axes = [list(range(n_bits))]
    orders = []
    for s in range(n_streams):
        turn = axes[s % len(axes):] + axes[:s % len(axes)]
        order = []
        for level in range(max(len(a) for a in turn)):
            order += [a[level] for a in turn if level < len(a)]
        orders.append(order)
    return orders


def hdot(left, right):
    return jnp.dot(left, right, precision=lax.Precision.HIGHEST)


def lower_blocks(rows):
    h = rows.shape[1] // 2
    left, right = rows[:, :h], rows[:, h:]
    return jnp.concatenate([hdot(left.T, left), hdot(right.T, left), hdot(right.T, right)], axis=0)


def right_solve_chol(blocks, rows):
    h = blocks.shape[1]
    eye = jnp.eye(h, dtype=blocks.dtype)
    l11 = jnp.linalg.cholesky(blocks[:h], symmetrize_input=False)
    i11 = jax.scipy.linalg.solve_triangular(l11, eye, lower=True)
    l21 = hdot(blocks[h:2 * h], i11.T)
    l22 = jnp.linalg.cholesky(blocks[2 * h:] - hdot(l21, l21.T), symmetrize_input=False)
    i22 = jax.scipy.linalg.solve_triangular(l22, eye, lower=True)
    x1 = hdot(rows[:, :h], i11.T)
    x2 = hdot(rows[:, h:] - hdot(x1, l21.T), i22.T)
    return jnp.concatenate([x1, x2], axis=1)


def local(hidden, routes, slots, down_weight, omega):
    n_exp = lax.axis_size("expert")
    n_dp = lax.axis_size("dp")
    tok_rows, n_route, hid_width = hidden.shape
    capacity = 2 * tok_rows * n_route // n_exp
    n_slot = n_exp * n_dp * capacity
    slot_index = (routes * capacity + slots).reshape(-1)
    one_hot = (
        slot_index[:, None] == lax.broadcasted_iota(jnp.int32, (1, n_exp * capacity), 1)
    ).astype(jnp.bfloat16)
    outgoing = contract(one_hot, hidden.reshape(-1, hid_width)).astype(jnp.bfloat16)
    outgoing = outgoing.reshape(n_exp, capacity, hid_width)
    received = lax.all_to_all(outgoing, "expert", split_axis=0, concat_axis=0, tiled=True).reshape(
        n_exp * capacity, hid_width
    )
    partner = lax.ppermute(received, "dp", [(0, 1), (1, 0)])
    gram_mat = (contract(received, received) + contract(partner, partner)) / n_slot
    on_diag = lax.broadcasted_iota(jnp.int32, gram_mat.shape, 0) == lax.broadcasted_iota(
        jnp.int32, gram_mat.shape, 1
    )
    diag_mean = jnp.sum(jnp.where(on_diag, gram_mat, 0.0)) / hid_width
    damped = jnp.where(on_diag, gram_mat + (damping * diag_mean + jitter), gram_mat)
    whitening = jnp.linalg.cholesky(damped, symmetrize_input=False)
    down_half = down_weight[0]
    half_cols = down_half.shape[1]
    def term(start, width):
        test_part = jnp.dot(
            whitening, omega[0, :, start:start + width].astype(jnp.float32),
            precision=lax.Precision.HIGHEST,
        ).astype(jnp.bfloat16)
        return contract(test_part, down_half)

    orders = bit_orders(n_exp, 2)
    sketch = scatter_sum(term, omega.shape[2], half_cols, orders)
    small_gram = all_sum(lower_blocks(sketch), orders[0])
    basis_rows = right_solve_chol(small_gram, sketch) * math.sqrt(half_cols * n_dp)
    own_rows = lax.dynamic_slice_in_dim(
        whitening, lax.axis_index("dp") * (hid_width // n_dp), hid_width // n_dp, 0
    )
    return (own_rows[None], basis_rows[None])


def solution(mesh):
    placed = (
        P(("expert", "dp"), None, None),
        P(("expert", "dp"), None),
        P(("expert", "dp"), None),
        P("expert", None, "dp"),
        P("expert", None, None),
    )
    return jax.shard_map(
        local,
        mesh=mesh,
        in_specs=placed,
        out_specs=(P("expert", "dp", None), P("dp", "expert", None)),
        check_vma=False,
    )
```
